256 devices in a mesh: dp: 32 (over x, z), tensor: 8 (over y, core).
Axes of the slice: x: 4, y: 4, z: 8, core: 2. Of those that a mesh axis runs over, the one named last changes fastest.
Arguments:
- counts: int32 [32], replicated, may hold values from 1 to 32, 512 in all
- keys: bfloat16 [1024, 28672], P('dp'), may hold values from -6 to 6
- inverse_cov: bfloat16 [28672, 28672], P('tensor', 'dp'), as said below
- hidden: bfloat16 [1024, 8192], P('dp', 'tensor'), may hold values from -6 to 6
- targets: bfloat16 [1024, 8192], P('dp', 'tensor'), may hold values from -48 to 48
- down_weight: bfloat16 [8192, 28672], P('tensor', 'dp'), may hold values from -0.03125 to 0.03125
Outputs:
- new_weight: bfloat16 [8192, 28672], P('tensor', 'dp')
- next_resid: bfloat16 [1024, 8192], P('dp', 'tensor')
The draws below stay inside these ranges and needn't reach their ends.
Inputs may be any that keep to these rules, and one draw needn't show every extreme that they name: Group g has counts[g] live edits in its first counts[g] slots; the counts sum to 512; some group holds 32. `inverse_cov`: symmetric positive definite.
All inputs are finite; a program needn't handle non-finite values.
Results may differ from the reference program's by a relative error of at most 0.01.
The reference program's roundings to bfloat16 on the way (of `masked_keys`, `precond`, `resid` and `solved`) count: a program that leaves them out, or rounds other values in their place, can miss the bound.
Values may be sent and summed in bfloat16 or wider, within the bound.
No kernel may reach another device: no remote copies, remote signals or barrier semaphores. Data moves between devices by JAX's collectives and lax.ppermute only.
A program may use at most 128 MiB of HBM per device.

```python
import math
import jax
import jax.numpy as jnp
import numpy as np
from jax import lax

D = 8192
FF = 28672
LAYERS_LEFT = 3
SLOTS = 32
ROWS = 1024
EDITS = 512
N_DP = 32


def draw_inverse_cov(key, part):
    key_base = jax.random.fold_in(key, 0)
    block_count = 32
    height = FF // block_count
    base_draw = jax.random.normal(key_base, (FF, FF), jnp.float32)
    coupling = 0.3 / math.sqrt(2.0 * FF)
    magnitude = 3.0 / FF

    def one_block(block_index):
        row_start = block_index * height
        row_block = lax.dynamic_slice_in_dim(base_draw, row_start, height, 0)
        col_block = lax.dynamic_slice_in_dim(base_draw, row_start, height, 1)
        symmetric = (row_block + col_block.T) * coupling
        row_ids = row_start + jnp.arange(height, dtype=jnp.int32)[:, None]
        col_ids = jnp.arange(FF, dtype=jnp.int32)[None, :]
        symmetric = symmetric + jnp.where(row_ids == col_ids, 1.0, 0.0)
        return (symmetric * magnitude).astype(jnp.bfloat16)
    return lax.map(one_block, jnp.arange(block_count, dtype=jnp.int32)).reshape(FF, FF)


def raised(result, key, source, target, shards_of, factor):
    def block_of(position):
        return (jnp.arange(result.shape[position]) // (result.shape[position] // shards_of)).reshape((-1,) + (1,) * (result.ndim - 1 - position))

    near = jax.random.permutation(key, shards_of)[block_of(target)]
    far = (block_of(target) + shards_of // 2) % shards_of
    return jnp.where((block_of(source) == near) | (block_of(source) == far), factor * result, result)


def block_levels(rng, dims, pieces, least, top_value):
    factor_of, own = 1.0, jax.random.fold_in(rng, 6)
    for position, blocks in pieces:
        steps = jnp.exp(jax.random.uniform(jax.random.fold_in(own, position), (blocks,), jnp.float32, least / len(pieces), top_value / len(pieces)))
        factor_of = factor_of * jnp.repeat(steps, dims[position] // blocks).reshape([-1 if axis == position else 1 for axis in range(len(dims))])
    return factor_of


def split_up(amount, total, bound, lean):
    weights = [(1 << 20) // math.isqrt(rank ** lean) + 1 for rank in range(2, amount + 1)]
    rest, given = total - bound - (amount - 1), [1] * (amount - 1)
    while rest > 0:
        movable = [i for i in range(amount - 1) if given[i] < bound]
        mass, left = sum([weights[i] for i in movable]), rest
        for i in movable:
            extra = min(bound - given[i], max(1, left * weights[i] // mass), rest)
            given[i] = given[i] + extra
            rest = rest - extra
    return np.array([bound] + given)


def uneven(key, count, total, most, skew):
    if count == 2:
        one = jax.random.randint(key, (), max(1, total - most), min(most, total - 1) + 1)
        return jnp.stack([one, total - one])
    tallies = jnp.asarray(split_up(count, total, most, skew), jnp.int32)
    couples = (count - 1) // 2
    donor, taker = tallies[1:1 + 2 * couples:2], tallies[2:2 + 2 * couples:2]
    margin = jnp.minimum(donor - 1, most - taker)
    shifted = jax.random.randint(jax.random.fold_in(key, 1), (couples,), 0, 1 << 20) % (margin + 1)
    tallies = tallies.at[1:1 + 2 * couples:2].set(donor - shifted).at[2:2 + 2 * couples:2].set(taker + shifted)
    return tallies[jax.random.permutation(jax.random.fold_in(key, 2), count)]


def gaussian(stream_key, extent, width, limit, shards=(), kind=jnp.bfloat16):
    values = jax.random.normal(stream_key, extent, jnp.float32) * width
    if len(shards) > 0:
        values = block_levels(stream_key, extent, shards, -0.22, 0.18) * values
    return jnp.clip(values, min=-limit, max=limit).astype(kind)


def noise_with(stream_key, shape, width, limit, cuts, heavy, kind=jnp.bfloat16):
    array = width * jax.random.normal(stream_key, shape, jnp.float32)
    if cuts:
        array = array * block_levels(stream_key, shape, cuts, -0.22, 0.18)
    return jnp.clip(raised(array, jax.random.fold_in(stream_key, 3), *heavy), -limit, limit).astype(kind)


def setup_inputs(seed: int = 0) -> dict:
    key_list = jax.random.split(jax.random.key(seed), 7)
    return {
        "counts": uneven(key_list[0], N_DP, EDITS, SLOTS, 2).astype(jnp.int32),
        "keys": noise_with(key_list[1], (ROWS, FF), 1.0, 6.0, ((0, 32),), (1, 0, 32, 2.75)),
        "inverse_cov": draw_inverse_cov(jax.random.fold_in(key_list[6], 71), 0),
        "hidden": gaussian(key_list[3], (ROWS, D), 1.0, 6.0, ((0, 32), (1, 8))),
        "targets": gaussian(key_list[4], (ROWS, D), 8.0, 48.0, ((0, 32), (1, 8))),
        "down_weight": gaussian(key_list[5], (D, FF), FF ** -0.5, 0.03125, ((0, 8), (1, 32))),
    }


def live_rows(counts):
    positions = jnp.arange(ROWS, dtype=jnp.int32)
    owners = (positions // SLOTS).astype(jnp.int32)
    return positions % SLOTS < jnp.take(counts, owners)

def cholesky_solve(system, right_side):
    factor = jnp.linalg.cholesky(system)
    middle = lax.linalg.triangular_solve(factor, right_side, left_side=True, lower=True)
    return lax.linalg.triangular_solve(factor, middle, left_side=True, lower=True, transpose_a=True)

def reference(counts, keys, inverse_cov, hidden, targets, down_weight):
    live_slot = live_rows(counts)[:, None]
    masked_keys = jnp.where(live_slot, keys, jnp.zeros_like(keys))
    precond = jnp.dot(masked_keys.astype(jnp.float32), inverse_cov.astype(jnp.float32), preferred_element_type=jnp.float32).astype(jnp.bfloat16)
    gram_matrix = jnp.dot(precond.astype(jnp.float32), masked_keys.T.astype(jnp.float32), preferred_element_type=jnp.float32)
    system = gram_matrix + jnp.eye(ROWS, dtype=jnp.float32)
    change = (targets.astype(jnp.float32) - hidden.astype(jnp.float32)) / LAYERS_LEFT
    resid = jnp.where(live_slot, change, jnp.zeros_like(change)).astype(jnp.bfloat16)
    solved = cholesky_solve(system, resid.astype(jnp.float32)).astype(jnp.bfloat16)
    weight_delta = jnp.dot(solved.T.astype(jnp.float32), precond.astype(jnp.float32), preferred_element_type=jnp.float32)
    new_weight = (down_weight.astype(jnp.float32) + weight_delta).astype(jnp.bfloat16)
    recomputed = jnp.dot(masked_keys.astype(jnp.float32), new_weight.T.astype(jnp.float32), preferred_element_type=jnp.float32)
    summed = hidden.astype(jnp.float32) + recomputed
    next_resid = jnp.where(live_slot, summed, jnp.zeros_like(summed)).astype(jnp.bfloat16)
    return (new_weight, next_resid)
```

```python
import jax
import jax.numpy as jnp
from jax import lax
from jax.sharding import PartitionSpec as P

LAYERS_LEFT = 3


def cholesky_solve(system, right_side):
    factor = jnp.linalg.cholesky(system)
    middle = lax.linalg.triangular_solve(factor, right_side, left_side=True, lower=True)
    return lax.linalg.triangular_solve(factor, middle, left_side=True, lower=True, transpose_a=True)


def rows_product(left, right):
    return lax.dot_general(
        left, right, (((1,), (1,)), ((), ())), preferred_element_type=jnp.float32
    )


def pick(select, values):
    return jnp.dot(select, values, preferred_element_type=jnp.float32).astype(values.dtype)


def per_device(counts, keys, inverse_cov, hidden, targets, down_weight):
    slot_count = keys.shape[0]
    group_size = lax.axis_size("dp")
    group_index = lax.axis_index("dp")
    tensor_index = lax.axis_index("tensor")
    width_part = inverse_cov.shape[0]
    row_total = slot_count * group_size
    live_total = row_total // 2

    ends = jnp.cumsum(counts)
    starts = ends - counts
    compact = jnp.arange(live_total, dtype=jnp.int32)
    owner = jnp.minimum(jnp.sum(compact[:, None] >= ends[None, :], axis=1), group_size - 1)
    row_of = owner * slot_count + compact - starts[owner]
    select = (row_of[:, None] == jnp.arange(row_total, dtype=jnp.int32)[None, :]).astype(jnp.bfloat16)

    slots = jnp.arange(slot_count, dtype=jnp.int32)
    live_vec = slots < counts[group_index]
    live_slot = live_vec[:, None]
    own_compact = jnp.where(live_vec, starts[group_index] + slots, 0)

    masked_keys = jnp.where(live_slot, keys, jnp.zeros_like(keys))
    column_part = lax.dynamic_slice_in_dim(masked_keys, tensor_index * width_part, width_part, 1)
    columns = lax.all_to_all(masked_keys, "dp", split_axis=1, concat_axis=0, tiled=True)
    gathered = lax.all_gather(column_part, "dp", axis=0, tiled=True)
    keys_c = pick(select, gathered)
    columns_c = pick(select, columns)
    partial_q = jnp.dot(keys_c, inverse_cov, preferred_element_type=jnp.float32)
    precond_c = lax.psum(partial_q, "tensor").astype(jnp.bfloat16)
    gram_c = lax.psum(rows_product(precond_c, columns_c), "dp")

    base_partial = rows_product(columns, down_weight)
    gram_c, base_partial = lax.optimization_barrier((gram_c, base_partial))
    base = lax.psum_scatter(base_partial, "dp", scatter_dimension=0, tiled=True)

    system = gram_c + jnp.eye(live_total, dtype=jnp.float32)
    change = (targets.astype(jnp.float32) - hidden.astype(jnp.float32)) / LAYERS_LEFT
    resid_local = jnp.where(live_slot, change, jnp.zeros_like(change)).astype(jnp.bfloat16)
    resid_all = lax.all_gather(resid_local, "dp", axis=0, tiled=True)
    resid_c = pick(select, resid_all)
    solved_c = cholesky_solve(system, resid_c.astype(jnp.float32)).astype(jnp.bfloat16)
    weight_delta = lax.dot_general(
        solved_c, precond_c, (((0,), (0,)), ((), ())), preferred_element_type=jnp.float32
    )
    new_weight = (down_weight.astype(jnp.float32) + weight_delta).astype(jnp.bfloat16)

    gram_own = jnp.where(live_slot, jnp.take(gram_c, own_compact, axis=1).T, 0.0)
    extra = jnp.dot(
        gram_own, solved_c.astype(jnp.float32),
        precision=lax.Precision.HIGHEST, preferred_element_type=jnp.float32,
    )
    summed = hidden.astype(jnp.float32) + (base + extra)
    next_resid = jnp.where(live_slot, summed, jnp.zeros_like(summed)).astype(jnp.bfloat16)
    return (new_weight, next_resid)


def solution(mesh):
    in_specs = (
        P(),
        P("dp", None),
        P("tensor", "dp"),
        P("dp", "tensor"),
        P("dp", "tensor"),
        P("tensor", "dp"),
    )
    out_specs = (P("tensor", "dp"), P("dp", "tensor"))
    return jax.shard_map(
        per_device, mesh=mesh, in_specs=in_specs, out_specs=out_specs, check_vma=False
    )
```

```python
import jax
import jax.numpy as jnp
from jax import lax
from jax.sharding import PartitionSpec as P

LAYERS_LEFT = 3


def cholesky_solve(system, right_side):
    factor = jnp.linalg.cholesky(system)
    middle = lax.linalg.triangular_solve(factor, right_side, left_side=True, lower=True)
    return lax.linalg.triangular_solve(factor, middle, left_side=True, lower=True, transpose_a=True)


def rows_product(left, right):
    return lax.dot_general(
        left, right, (((1,), (1,)), ((), ())), preferred_element_type=jnp.float32
    )


def pick(select, values):
    return jnp.dot(select, values, preferred_element_type=jnp.float32).astype(values.dtype)


def gather_rows(x, axis):
    n = lax.axis_size(axis)
    copies = jnp.broadcast_to(x[None], (n,) + x.shape)
    return lax.all_to_all(copies, axis, 0, 0, tiled=True).reshape((n * x.shape[0],) + x.shape[1:])


def scatter_rows_sum(x, axis):
    n = lax.axis_size(axis)
    parts = lax.all_to_all(x.reshape((n, x.shape[0] // n) + x.shape[1:]), axis, 0, 0, tiled=True)
    return parts.sum(0)


def per_device(counts, keys, inverse_cov, hidden, targets, down_weight):
    slot_count = keys.shape[0]
    group_size = lax.axis_size("dp")
    group_index = lax.axis_index("dp")
    tensor_index = lax.axis_index("tensor")
    width_part = inverse_cov.shape[0]
    row_total = slot_count * group_size
    live_total = row_total // 2

    ends = jnp.cumsum(counts)
    starts = ends - counts
    compact = jnp.arange(live_total, dtype=jnp.int32)
    owner = jnp.minimum(jnp.sum(compact[:, None] >= ends[None, :], axis=1), group_size - 1)
    row_of = owner * slot_count + compact - starts[owner]
    select = (row_of[:, None] == jnp.arange(row_total, dtype=jnp.int32)[None, :]).astype(jnp.bfloat16)

    slots = jnp.arange(slot_count, dtype=jnp.int32)
    live_vec = slots < counts[group_index]
    live_slot = live_vec[:, None]
    own_compact = jnp.where(live_vec, starts[group_index] + slots, 0)

    masked_keys = jnp.where(live_slot, keys, jnp.zeros_like(keys))
    column_part = lax.dynamic_slice_in_dim(masked_keys, tensor_index * width_part, width_part, 1)
    columns = lax.all_to_all(masked_keys, "dp", split_axis=1, concat_axis=0, tiled=True)
    gathered = lax.all_gather(column_part, "dp", axis=0, tiled=True)
    keys_c = pick(select, gathered)
    columns_c = pick(select, columns)
    partial_q = jnp.dot(keys_c, inverse_cov, preferred_element_type=jnp.float32)
    precond_c = gather_rows(scatter_rows_sum(partial_q, "tensor").astype(jnp.bfloat16), "tensor")
    gram_c = gather_rows(scatter_rows_sum(rows_product(precond_c, columns_c), "dp"), "dp")

    base_partial = rows_product(columns, down_weight)
    gram_c, base_partial = lax.optimization_barrier((gram_c, base_partial))
    base = scatter_rows_sum(base_partial, "dp")

    system = gram_c + jnp.eye(live_total, dtype=jnp.float32)
    change = (targets.astype(jnp.float32) - hidden.astype(jnp.float32)) / LAYERS_LEFT
    resid_local = jnp.where(live_slot, change, jnp.zeros_like(change)).astype(jnp.bfloat16)
    resid_all = lax.all_gather(resid_local, "dp", axis=0, tiled=True)
    resid_c = pick(select, resid_all)
    solved_c = cholesky_solve(system, resid_c.astype(jnp.float32)).astype(jnp.bfloat16)
    weight_delta = lax.dot_general(
        solved_c, precond_c, (((0,), (0,)), ((), ())), preferred_element_type=jnp.float32
    )
    new_weight = (down_weight.astype(jnp.float32) + weight_delta).astype(jnp.bfloat16)

    gram_own = jnp.where(live_slot, jnp.take(gram_c, own_compact, axis=1).T, 0.0)
    extra = jnp.dot(
        gram_own, solved_c.astype(jnp.float32),
        precision=lax.Precision.HIGHEST, preferred_element_type=jnp.float32,
    )
    summed = hidden.astype(jnp.float32) + (base + extra)
    next_resid = jnp.where(live_slot, summed, jnp.zeros_like(summed)).astype(jnp.bfloat16)
    return (new_weight, next_resid)


def solution(mesh):
    in_specs = (
        P(),
        P("dp", None),
        P("tensor", "dp"),
        P("dp", "tensor"),
        P("dp", "tensor"),
        P("tensor", "dp"),
    )
    out_specs = (P("tensor", "dp"), P("dp", "tensor"))
    return jax.shard_map(
        per_device, mesh=mesh, in_specs=in_specs, out_specs=out_specs, check_vma=False
    )
```

```python
import jax
import jax.numpy as jnp
from jax import lax
from jax.sharding import PartitionSpec as P

LAYERS_LEFT = 3


def cholesky_solve(system, right_side):
    factor = jnp.linalg.cholesky(system)
    middle = lax.linalg.triangular_solve(factor, right_side, left_side=True, lower=True)
    return lax.linalg.triangular_solve(factor, middle, left_side=True, lower=True, transpose_a=True)


def rows_product(left, right):
    return lax.dot_general(
        left, right, (((1,), (1,)), ((), ())), preferred_element_type=jnp.float32
    )


def pick(select, values):
    return jnp.dot(select, values, preferred_element_type=jnp.float32).astype(values.dtype)


def gather_rows(x, axis):
    n = lax.axis_size(axis)
    copies = jnp.broadcast_to(x[None], (n,) + x.shape)
    return lax.all_to_all(copies, axis, 0, 0, tiled=True).reshape((n * x.shape[0],) + x.shape[1:])


def scatter_rows_sum(x, axis):
    n = lax.axis_size(axis)
    parts = lax.all_to_all(x.reshape((n, x.shape[0] // n) + x.shape[1:]), axis, 0, 0, tiled=True)
    return parts.sum(0)


def per_device(counts, keys, inverse_cov, hidden, targets, down_weight):
    slot_count = keys.shape[0]
    group_size = lax.axis_size("dp")
    group_index = lax.axis_index("dp")
    tensor_index = lax.axis_index("tensor")
    width_part = inverse_cov.shape[0]
    row_total = slot_count * group_size
    live_total = row_total // 2

    ends = jnp.cumsum(counts)
    starts = ends - counts
    compact = jnp.arange(live_total, dtype=jnp.int32)
    owner = jnp.minimum(jnp.sum(compact[:, None] >= ends[None, :], axis=1), group_size - 1)
    row_of = owner * slot_count + compact - starts[owner]
    select = (row_of[:, None] == jnp.arange(row_total, dtype=jnp.int32)[None, :]).astype(jnp.bfloat16)

    slots = jnp.arange(slot_count, dtype=jnp.int32)
    live_vec = slots < counts[group_index]
    live_slot = live_vec[:, None]
    own_compact = jnp.where(live_vec, starts[group_index] + slots, 0)

    masked_keys = jnp.where(live_slot, keys, jnp.zeros_like(keys))
    column_part = lax.dynamic_slice_in_dim(masked_keys, tensor_index * width_part, width_part, 1)
    columns = lax.all_to_all(masked_keys, "dp", split_axis=1, concat_axis=0, tiled=True)
    gathered = lax.all_gather(column_part, "dp", axis=0, tiled=True)
    change = (targets.astype(jnp.float32) - hidden.astype(jnp.float32)) / LAYERS_LEFT
    resid_local = jnp.where(live_slot, change, jnp.zeros_like(change)).astype(jnp.bfloat16)
    resid_all = gather_rows(resid_local, "dp")
    gathered, columns, resid_all = lax.optimization_barrier((gathered, columns, resid_all))
    keys_c = pick(select, gathered)
    columns_c = pick(select, columns)
    partial_q = jnp.dot(keys_c, inverse_cov, preferred_element_type=jnp.float32)
    precond_c = gather_rows(scatter_rows_sum(partial_q, "tensor").astype(jnp.bfloat16), "tensor")
    gram_c = gather_rows(scatter_rows_sum(rows_product(precond_c, columns_c), "dp"), "dp")

    base_partial = rows_product(columns, down_weight)
    gram_c, base_partial = lax.optimization_barrier((gram_c, base_partial))
    base = scatter_rows_sum(base_partial, "dp")

    system = gram_c + jnp.eye(live_total, dtype=jnp.float32)
    resid_c = pick(select, resid_all)
    solved_c = cholesky_solve(system, resid_c.astype(jnp.float32)).astype(jnp.bfloat16)
    weight_delta = lax.dot_general(
        solved_c, precond_c, (((0,), (0,)), ((), ())), preferred_element_type=jnp.float32
    )
    new_weight = (down_weight.astype(jnp.float32) + weight_delta).astype(jnp.bfloat16)

    gram_own = jnp.where(live_slot, jnp.take(gram_c, own_compact, axis=1).T, 0.0)
    extra = jnp.dot(
        gram_own, solved_c.astype(jnp.float32),
        precision=lax.Precision.HIGHEST, preferred_element_type=jnp.float32,
    )
    summed = hidden.astype(jnp.float32) + (base + extra)
    next_resid = jnp.where(live_slot, summed, jnp.zeros_like(summed)).astype(jnp.bfloat16)
    return (new_weight, next_resid)


def solution(mesh):
    in_specs = (
        P(),
        P("dp", None),
        P("tensor", "dp"),
        P("dp", "tensor"),
        P("dp", "tensor"),
        P("tensor", "dp"),
    )
    out_specs = (P("tensor", "dp"), P("dp", "tensor"))
    return jax.shard_map(
        per_device, mesh=mesh, in_specs=in_specs, out_specs=out_specs, check_vma=False
    )
```

```python
import jax
import jax.numpy as jnp
from jax import lax
from jax.sharding import PartitionSpec as P

LAYERS_LEFT = 3


def cholesky_solve(system, right_side):
    factor = jnp.linalg.cholesky(system)
    middle = lax.linalg.triangular_solve(factor, right_side, left_side=True, lower=True)
    return lax.linalg.triangular_solve(factor, middle, left_side=True, lower=True, transpose_a=True)


def rows_product(left, right):
    return lax.dot_general(
        left, right, (((1,), (1,)), ((), ())), preferred_element_type=jnp.float32
    )


def pick(select, values):
    return jnp.dot(select, values, preferred_element_type=jnp.float32).astype(values.dtype)


def gather_rows(x, axis):
    n = lax.axis_size(axis)
    copies = jnp.broadcast_to(x[None], (n,) + x.shape)
    return lax.all_to_all(copies, axis, 0, 0, tiled=True).reshape((n * x.shape[0],) + x.shape[1:])


def scatter_rows_sum(x, axis):
    n = lax.axis_size(axis)
    parts = lax.all_to_all(x.reshape((n, x.shape[0] // n) + x.shape[1:]), axis, 0, 0, tiled=True)
    return parts.sum(0)


def per_device(counts, keys, inverse_cov, hidden, targets, down_weight):
    slot_count = keys.shape[0]
    group_size = lax.axis_size("dp")
    group_index = lax.axis_index("dp")
    tensor_index = lax.axis_index("tensor")
    width_part = inverse_cov.shape[0]
    row_total = slot_count * group_size
    live_total = row_total // 2

    ends = jnp.cumsum(counts)
    starts = ends - counts
    compact = jnp.arange(live_total, dtype=jnp.int32)
    owner = jnp.minimum(jnp.sum(compact[:, None] >= ends[None, :], axis=1), group_size - 1)
    row_of = owner * slot_count + compact - starts[owner]
    select = (row_of[:, None] == jnp.arange(row_total, dtype=jnp.int32)[None, :]).astype(jnp.bfloat16)

    slots = jnp.arange(slot_count, dtype=jnp.int32)
    live_vec = slots < counts[group_index]
    live_slot = live_vec[:, None]
    own_compact = jnp.where(live_vec, starts[group_index] + slots, 0)

    masked_keys = jnp.where(live_slot, keys, jnp.zeros_like(keys))
    column_part = lax.dynamic_slice_in_dim(masked_keys, tensor_index * width_part, width_part, 1)
    columns = lax.all_to_all(masked_keys, "dp", split_axis=1, concat_axis=0, tiled=True)
    gathered = lax.all_gather(column_part, "dp", axis=0, tiled=True)
    change = (targets.astype(jnp.float32) - hidden.astype(jnp.float32)) / LAYERS_LEFT
    resid_local = jnp.where(live_slot, change, jnp.zeros_like(change)).astype(jnp.bfloat16)
    gathered, columns = lax.optimization_barrier((gathered, columns))
    resid_all = lax.all_gather(resid_local, "dp", axis=0, tiled=True)
    keys_c = pick(select, gathered)
    columns_c = pick(select, columns)
    partial_q = jnp.dot(keys_c, inverse_cov, preferred_element_type=jnp.float32)
    precond_c = gather_rows(scatter_rows_sum(partial_q, "tensor").astype(jnp.bfloat16), "tensor")
    gram_c = gather_rows(scatter_rows_sum(rows_product(precond_c, columns_c), "dp"), "dp")

    base_partial = rows_product(columns, down_weight)
    gram_c, base_partial = lax.optimization_barrier((gram_c, base_partial))
    base = scatter_rows_sum(base_partial, "dp")

    system = gram_c + jnp.eye(live_total, dtype=jnp.float32)
    resid_c = pick(select, resid_all)
    solved_c = cholesky_solve(system, resid_c.astype(jnp.float32)).astype(jnp.bfloat16)
    weight_delta = lax.dot_general(
        solved_c, precond_c, (((0,), (0,)), ((), ())), preferred_element_type=jnp.float32
    )
    new_weight = (down_weight.astype(jnp.float32) + weight_delta).astype(jnp.bfloat16)

    gram_own = jnp.where(live_slot, jnp.take(gram_c, own_compact, axis=1).T, 0.0)
    extra = jnp.dot(
        gram_own, solved_c.astype(jnp.float32),
        precision=lax.Precision.HIGHEST, preferred_element_type=jnp.float32,
    )
    summed = hidden.astype(jnp.float32) + (base + extra)
    next_resid = jnp.where(live_slot, summed, jnp.zeros_like(summed)).astype(jnp.bfloat16)
    return (new_weight, next_resid)


def solution(mesh):
    in_specs = (
        P(),
        P("dp", None),
        P("tensor", "dp"),
        P("dp", "tensor"),
        P("dp", "tensor"),
        P("tensor", "dp"),
    )
    out_specs = (P("tensor", "dp"), P("dp", "tensor"))
    return jax.shard_map(
        per_device, mesh=mesh, in_specs=in_specs, out_specs=out_specs, check_vma=False
    )
```

```python
import jax
import jax.numpy as jnp
from jax import lax
from jax.sharding import PartitionSpec as P

LAYERS_LEFT = 3


def cholesky_solve(system, right_side):
    factor = jnp.linalg.cholesky(system)
    middle = lax.linalg.triangular_solve(factor, right_side, left_side=True, lower=True)
    return lax.linalg.triangular_solve(factor, middle, left_side=True, lower=True, transpose_a=True)


def rows_product(left, right):
    return lax.dot_general(
        left, right, (((1,), (1,)), ((), ())), preferred_element_type=jnp.float32
    )


def pick(select, values):
    return jnp.dot(select, values, preferred_element_type=jnp.float32).astype(values.dtype)


def gather_rows(x, axis):
    n = lax.axis_size(axis)
    copies = jnp.broadcast_to(x[None], (n,) + x.shape)
    return lax.all_to_all(copies, axis, 0, 0, tiled=True).reshape((n * x.shape[0],) + x.shape[1:])


def scatter_rows_sum(x, axis):
    n = lax.axis_size(axis)
    parts = lax.all_to_all(x.reshape((n, x.shape[0] // n) + x.shape[1:]), axis, 0, 0, tiled=True)
    return parts.sum(0)


def per_device(counts, keys, inverse_cov, hidden, targets, down_weight):
    slot_count = keys.shape[0]
    group_size = lax.axis_size("dp")
    group_index = lax.axis_index("dp")
    tensor_index = lax.axis_index("tensor")
    width_part = inverse_cov.shape[0]
    row_total = slot_count * group_size
    live_total = row_total // 2

    ends = jnp.cumsum(counts)
    starts = ends - counts
    compact = jnp.arange(live_total, dtype=jnp.int32)
    owner = jnp.minimum(jnp.sum(compact[:, None] >= ends[None, :], axis=1), group_size - 1)
    row_of = owner * slot_count + compact - starts[owner]
    select = (row_of[:, None] == jnp.arange(row_total, dtype=jnp.int32)[None, :]).astype(jnp.bfloat16)

    slots = jnp.arange(slot_count, dtype=jnp.int32)
    live_vec = slots < counts[group_index]
    live_slot = live_vec[:, None]
    own_compact = jnp.where(live_vec, starts[group_index] + slots, 0)

    masked_keys = jnp.where(live_slot, keys, jnp.zeros_like(keys))
    column_part = lax.dynamic_slice_in_dim(masked_keys, tensor_index * width_part, width_part, 1)
    columns = lax.all_to_all(masked_keys, "dp", split_axis=1, concat_axis=0, tiled=True)
    gathered = lax.all_gather(column_part, "dp", axis=0, tiled=True)
    change = (targets.astype(jnp.float32) - hidden.astype(jnp.float32)) / LAYERS_LEFT
    resid_local = jnp.where(live_slot, change, jnp.zeros_like(change)).astype(jnp.bfloat16)
    gathered, columns = lax.optimization_barrier((gathered, columns))
    resid_all = lax.all_gather(resid_local, "dp", axis=0, tiled=True)
    keys_c = pick(select, gathered)
    columns_c = pick(select, columns)
    partial_q = jnp.dot(keys_c, inverse_cov, preferred_element_type=jnp.float32)
    precond_c = gather_rows(scatter_rows_sum(partial_q, "tensor").astype(jnp.bfloat16), "tensor")
    gram_c = gather_rows(scatter_rows_sum(rows_product(precond_c, columns_c), "dp"), "dp")

    base_partial = rows_product(columns, down_weight)
    gram_c, base_partial = lax.optimization_barrier((gram_c, base_partial))
    base = scatter_rows_sum(base_partial, "dp")

    system = gram_c + jnp.eye(live_total, dtype=jnp.float32)
    factor = jnp.linalg.cholesky(system)
    factor, resid_all = lax.optimization_barrier((factor, resid_all))
    resid_c = pick(select, resid_all)
    middle = lax.linalg.triangular_solve(factor, resid_c.astype(jnp.float32), left_side=True, lower=True)
    solved_c = lax.linalg.triangular_solve(
        factor, middle, left_side=True, lower=True, transpose_a=True
    ).astype(jnp.bfloat16)
    weight_delta = lax.dot_general(
        solved_c, precond_c, (((0,), (0,)), ((), ())), preferred_element_type=jnp.float32
    )
    new_weight = (down_weight.astype(jnp.float32) + weight_delta).astype(jnp.bfloat16)

    gram_own = jnp.where(live_slot, jnp.take(gram_c, own_compact, axis=1).T, 0.0)
    extra = jnp.dot(
        gram_own, solved_c.astype(jnp.float32),
        precision=lax.Precision.HIGHEST, preferred_element_type=jnp.float32,
    )
    summed = hidden.astype(jnp.float32) + (base + extra)
    next_resid = jnp.where(live_slot, summed, jnp.zeros_like(summed)).astype(jnp.bfloat16)
    return (new_weight, next_resid)


def solution(mesh):
    in_specs = (
        P(),
        P("dp", None),
        P("tensor", "dp"),
        P("dp", "tensor"),
        P("dp", "tensor"),
        P("tensor", "dp"),
    )
    out_specs = (P("tensor", "dp"), P("dp", "tensor"))
    return jax.shard_map(
        per_device, mesh=mesh, in_specs=in_specs, out_specs=out_specs, check_vma=False
    )
```

```python
import jax
import jax.numpy as jnp
from jax import lax
from jax.sharding import PartitionSpec as P

LAYERS_LEFT = 3


def cholesky_solve(system, right_side):
    factor = jnp.linalg.cholesky(system)
    middle = lax.linalg.triangular_solve(factor, right_side, left_side=True, lower=True)
    return lax.linalg.triangular_solve(factor, middle, left_side=True, lower=True, transpose_a=True)


def rows_product(left, right):
    return lax.dot_general(
        left, right, (((1,), (1,)), ((), ())), preferred_element_type=jnp.float32
    )


def pick(select, values):
    return jnp.dot(select, values, preferred_element_type=jnp.float32).astype(values.dtype)


def gather_rows(x, axis):
    n = lax.axis_size(axis)
    copies = jnp.broadcast_to(x[None], (n,) + x.shape)
    return lax.all_to_all(copies, axis, 0, 0, tiled=True).reshape((n * x.shape[0],) + x.shape[1:])


def scatter_rows_sum(x, axis):
    n = lax.axis_size(axis)
    parts = lax.all_to_all(x.reshape((n, x.shape[0] // n) + x.shape[1:]), axis, 0, 0, tiled=True)
    return parts.sum(0)


def per_device(counts, keys, inverse_cov, hidden, targets, down_weight):
    slot_count = keys.shape[0]
    group_size = lax.axis_size("dp")
    group_index = lax.axis_index("dp")
    tensor_index = lax.axis_index("tensor")
    width_part = inverse_cov.shape[0]
    row_total = slot_count * group_size
    live_total = row_total // 2

    ends = jnp.cumsum(counts)
    starts = ends - counts
    compact = jnp.arange(live_total, dtype=jnp.int32)
    owner = jnp.minimum(jnp.sum(compact[:, None] >= ends[None, :], axis=1), group_size - 1)
    row_of = owner * slot_count + compact - starts[owner]
    select = (row_of[:, None] == jnp.arange(row_total, dtype=jnp.int32)[None, :]).astype(jnp.bfloat16)

    slots = jnp.arange(slot_count, dtype=jnp.int32)
    live_vec = slots < counts[group_index]
    live_slot = live_vec[:, None]
    own_compact = jnp.where(live_vec, starts[group_index] + slots, 0)

    masked_keys = jnp.where(live_slot, keys, jnp.zeros_like(keys))
    column_part = lax.dynamic_slice_in_dim(masked_keys, tensor_index * width_part, width_part, 1)
    columns = lax.all_to_all(masked_keys, "dp", split_axis=1, concat_axis=0, tiled=True)
    gathered = lax.all_gather(column_part, "dp", axis=0, tiled=True)
    change = (targets.astype(jnp.float32) - hidden.astype(jnp.float32)) / LAYERS_LEFT
    resid_local = jnp.where(live_slot, change, jnp.zeros_like(change)).astype(jnp.bfloat16)
    gathered, columns = lax.optimization_barrier((gathered, columns))
    keys_c = pick(select, gathered)
    columns_c = pick(select, columns)
    partial_q = jnp.dot(keys_c, inverse_cov, preferred_element_type=jnp.float32)
    precond_c = gather_rows(scatter_rows_sum(partial_q, "tensor").astype(jnp.bfloat16), "tensor")
    gram_c = gather_rows(scatter_rows_sum(rows_product(precond_c, columns_c), "dp"), "dp")

    base_partial = rows_product(columns, down_weight)
    gram_c, base_partial, resid_local = lax.optimization_barrier((gram_c, base_partial, resid_local))
    resid_all = lax.all_gather(resid_local, "dp", axis=0, tiled=True)
    base = scatter_rows_sum(base_partial, "dp")

    system = gram_c + jnp.eye(live_total, dtype=jnp.float32)
    factor = jnp.linalg.cholesky(system)
    factor, resid_all = lax.optimization_barrier((factor, resid_all))
    resid_c = pick(select, resid_all)
    middle = lax.linalg.triangular_solve(factor, resid_c.astype(jnp.float32), left_side=True, lower=True)
    solved_c = lax.linalg.triangular_solve(
        factor, middle, left_side=True, lower=True, transpose_a=True
    ).astype(jnp.bfloat16)
    weight_delta = lax.dot_general(
        solved_c, precond_c, (((0,), (0,)), ((), ())), preferred_element_type=jnp.float32
    )
    new_weight = (down_weight.astype(jnp.float32) + weight_delta).astype(jnp.bfloat16)

    gram_own = jnp.where(live_slot, jnp.take(gram_c, own_compact, axis=1).T, 0.0)
    extra = jnp.dot(
        gram_own, solved_c.astype(jnp.float32),
        precision=lax.Precision.HIGHEST, preferred_element_type=jnp.float32,
    )
    summed = hidden.astype(jnp.float32) + (base + extra)
    next_resid = jnp.where(live_slot, summed, jnp.zeros_like(summed)).astype(jnp.bfloat16)
    return (new_weight, next_resid)


def solution(mesh):
    in_specs = (
        P(),
        P("dp", None),
        P("tensor", "dp"),
        P("dp", "tensor"),
        P("dp", "tensor"),
        P("tensor", "dp"),
    )
    out_specs = (P("tensor", "dp"), P("dp", "tensor"))
    return jax.shard_map(
        per_device, mesh=mesh, in_specs=in_specs, out_specs=out_specs, check_vma=False
    )
```

```python
import jax
import jax.numpy as jnp
from jax import lax
from jax.sharding import PartitionSpec as P

LAYERS_LEFT = 3


def cholesky_solve(system, right_side):
    factor = jnp.linalg.cholesky(system)
    middle = lax.linalg.triangular_solve(factor, right_side, left_side=True, lower=True)
    return lax.linalg.triangular_solve(factor, middle, left_side=True, lower=True, transpose_a=True)


def rows_product(left, right):
    return lax.dot_general(
        left, right, (((1,), (1,)), ((), ())), preferred_element_type=jnp.float32
    )


def pick(select, values):
    return jnp.dot(select, values, preferred_element_type=jnp.float32).astype(values.dtype)


def gather_rows(x, axis):
    n = lax.axis_size(axis)
    copies = jnp.broadcast_to(x[None], (n,) + x.shape)
    return lax.all_to_all(copies, axis, 0, 0, tiled=True).reshape((n * x.shape[0],) + x.shape[1:])


def scatter_rows_sum(x, axis):
    n = lax.axis_size(axis)
    parts = lax.all_to_all(x.reshape((n, x.shape[0] // n) + x.shape[1:]), axis, 0, 0, tiled=True)
    return parts.sum(0)


def per_device(counts, keys, inverse_cov, hidden, targets, down_weight):
    slot_count = keys.shape[0]
    group_size = lax.axis_size("dp")
    group_index = lax.axis_index("dp")
    tensor_index = lax.axis_index("tensor")
    width_part = inverse_cov.shape[0]
    row_total = slot_count * group_size
    live_total = row_total // 2

    ends = jnp.cumsum(counts)
    starts = ends - counts
    compact = jnp.arange(live_total, dtype=jnp.int32)
    owner = jnp.minimum(jnp.sum(compact[:, None] >= ends[None, :], axis=1), group_size - 1)
    row_of = owner * slot_count + compact - starts[owner]
    select = (row_of[:, None] == jnp.arange(row_total, dtype=jnp.int32)[None, :]).astype(jnp.bfloat16)

    slots = jnp.arange(slot_count, dtype=jnp.int32)
    live_vec = slots < counts[group_index]
    live_slot = live_vec[:, None]
    own_compact = jnp.where(live_vec, starts[group_index] + slots, 0)

    masked_keys = jnp.where(live_slot, keys, jnp.zeros_like(keys))
    column_part = lax.dynamic_slice_in_dim(masked_keys, tensor_index * width_part, width_part, 1)
    columns = lax.all_to_all(masked_keys, "dp", split_axis=1, concat_axis=0, tiled=True)
    gathered = lax.all_gather(column_part, "dp", axis=0, tiled=True)
    change = (targets.astype(jnp.float32) - hidden.astype(jnp.float32)) / LAYERS_LEFT
    resid_local = jnp.where(live_slot, change, jnp.zeros_like(change)).astype(jnp.bfloat16)
    gathered, columns = lax.optimization_barrier((gathered, columns))
    resid_all = lax.all_gather(resid_local, "dp", axis=0, tiled=True)
    keys_c = pick(select, gathered)
    columns_c = pick(select, columns)
    partial_q = jnp.dot(keys_c, inverse_cov, preferred_element_type=jnp.float32)
    tensor_size = lax.axis_size("tensor")
    parts_q = lax.all_to_all(
        partial_q.astype(jnp.bfloat16).reshape((tensor_size, -1) + partial_q.shape[1:]),
        "tensor", 0, 0, tiled=True,
    ).astype(jnp.float32).sum(0)
    precond_c = gather_rows(parts_q.astype(jnp.bfloat16), "tensor")
    gram_c = gather_rows(scatter_rows_sum(rows_product(precond_c, columns_c), "dp"), "dp")

    base_partial = rows_product(columns, down_weight)
    gram_c, base_partial = lax.optimization_barrier((gram_c, base_partial))
    base = scatter_rows_sum(base_partial, "dp")

    system = gram_c + jnp.eye(live_total, dtype=jnp.float32)
    factor = jnp.linalg.cholesky(system)
    factor, resid_all = lax.optimization_barrier((factor, resid_all))
    resid_c = pick(select, resid_all)
    middle = lax.linalg.triangular_solve(factor, resid_c.astype(jnp.float32), left_side=True, lower=True)
    solved_c = lax.linalg.triangular_solve(
        factor, middle, left_side=True, lower=True, transpose_a=True
    ).astype(jnp.bfloat16)
    weight_delta = lax.dot_general(
        solved_c, precond_c, (((0,), (0,)), ((), ())), preferred_element_type=jnp.float32
    )
    new_weight = (down_weight.astype(jnp.float32) + weight_delta).astype(jnp.bfloat16)

    gram_own = jnp.where(live_slot, jnp.take(gram_c, own_compact, axis=1).T, 0.0)
    extra = jnp.dot(
        gram_own, solved_c.astype(jnp.float32),
        precision=lax.Precision.HIGHEST, preferred_element_type=jnp.float32,
    )
    summed = hidden.astype(jnp.float32) + (base + extra)
    next_resid = jnp.where(live_slot, summed, jnp.zeros_like(summed)).astype(jnp.bfloat16)
    return (new_weight, next_resid)


def solution(mesh):
    in_specs = (
        P(),
        P("dp", None),
        P("tensor", "dp"),
        P("dp", "tensor"),
        P("dp", "tensor"),
        P("tensor", "dp"),
    )
    out_specs = (P("tensor", "dp"), P("dp", "tensor"))
    return jax.shard_map(
        per_device, mesh=mesh, in_specs=in_specs, out_specs=out_specs, check_vma=False
    )
```
